1024 devices in a mesh: ctx: 64 (over y, x, z_hi, core), tp: 16 (over z_lo).
Axes of the slice: x: 4, y: 4, z: 32 (z_hi: 2, z_lo: 16; z = z_hi * 16 + z_lo), core: 2. Of those that a mesh axis runs over, the one named last changes fastest.
Arguments:
- query_stream: bfloat16 [16384, 8192], P('ctx', 'tp'), may hold values from -6 to 6
- key_stream: bfloat16 [16384, 8192], P('ctx', 'tp'), may hold values from -6 to 6
- value_stream: bfloat16 [16384, 8192], P('ctx', 'tp'), may hold values from -6 to 6
- feat_taps: float32 [3, 7, 8192], P(None, None, 'tp'), may hold values from -2 to 2
- filt_taps: float32 [128, 8192], P(None, 'tp'), may hold values from -0.5 to 0.5
- skip_bias: float32 [8192], P('tp'), may hold values from -3 to 3
- out_weight: bfloat16 [8192, 8192], P('tp'), may hold values from -0.09375 to 0.09375
Outputs:
- block_out: bfloat16 [16384, 8192], P('ctx', 'tp')
The draws below stay inside these ranges and needn't reach their ends.
All inputs are finite; a program needn't handle non-finite values.
Results may differ from the reference program's by a relative error of at most 0.02.
Values may be sent and summed in bfloat16 or wider, within the bound.
No kernel may reach another device: no remote copies, remote signals or barrier semaphores. Data moves between devices by JAX's collectives and lax.ppermute only.
A program may use at most 32 MiB of HBM per device.

```python
import jax
import jax.numpy as jnp
from jax import lax

D = 8192
TAPS = 128
FEAT = 7
LENGTH = 16384
N_TP = 16


def with_spikes(array, own_key, source, target, blocks, factor):
    def block_of(axis_at):
        return (jnp.arange(array.shape[axis_at]) // (array.shape[axis_at] // blocks)).reshape((-1,) + (1,) * (array.ndim - 1 - axis_at))

    near = jax.random.permutation(own_key, blocks)[block_of(target)]
    other_side = (block_of(target) + blocks // 2) % blocks
    return jnp.where((block_of(source) == near) | (block_of(source) == other_side), factor * array, array)


def shard_levels(rng, shape, pieces, smallest, top_value):
    factor_of, own = 1.0, jax.random.fold_in(rng, 6)
    for dim, parts in pieces:
        steps = jnp.exp(jax.random.uniform(jax.random.fold_in(own, dim), (parts,), jnp.float32, smallest / len(pieces), top_value / len(pieces)))
        factor_of = factor_of * jnp.repeat(steps, shape[dim] // parts).reshape([-1 if axis == dim else 1 for axis in range(len(shape))])
    return factor_of


def centred(rng, extent, width, bound, shards=(), held_as=jnp.bfloat16):
    factor_of = shard_levels(rng, extent, shards, -0.22, 0.18) if shards else 1.0
    values = jax.random.normal(rng, extent, jnp.float32) * width * factor_of
    return jnp.minimum(jnp.maximum(values, -bound), bound).astype(held_as)


def noise_with(own_key, dims, spread, bound, pieces, heavy, kind=jnp.bfloat16):
    result = spread * jax.random.normal(own_key, dims, jnp.float32)
    if pieces:
        result = result * shard_levels(own_key, dims, pieces, -0.22, 0.18)
    return jnp.clip(with_spikes(result, jax.random.fold_in(own_key, 3), *heavy), -bound, bound).astype(kind)


def setup_inputs(seed: int = 0) -> dict:
    keys = jax.random.split(jax.random.key(seed), 8)
    query_stream = centred(keys[0], (LENGTH, D), 1.0, 6.0, ((0, 64), (1, 16)))
    key_stream = centred(keys[1], (LENGTH, D), 1.0, 6.0, ((0, 64), (1, 16)))
    value_stream = centred(keys[2], (LENGTH, D), 1.0, 6.0, ((0, 64), (1, 16)))
    feat_taps = centred(keys[3], (3, FEAT, D), FEAT ** -0.5, 2.0, ((2, 16),), jnp.float32)
    filt_taps = centred(keys[4], (TAPS, D), TAPS ** -0.5, 0.5, ((1, 16),), jnp.float32)
    skip_bias = centred(keys[5], (D,), 0.5, 3.0, ((0, 16),), jnp.float32)
    out_weight = noise_with(keys[6], (D, D), D ** -0.5, 0.09375, ((0, 16),), (0, 1, 16, 2.0))
    return dict(query_stream=query_stream, key_stream=key_stream, value_stream=value_stream, feat_taps=feat_taps, filt_taps=filt_taps, skip_bias=skip_bias, out_weight=out_weight)


def causal_conv(signal, taps):
    tap_count = taps.shape[0]
    seq_len = signal.shape[0]
    padded = jnp.concatenate([jnp.zeros((tap_count - 1, signal.shape[1]), signal.dtype), signal], 0)

    def add_tap(offset, running):
        window = lax.dynamic_slice_in_dim(padded, (tap_count - 1 - offset).astype(jnp.int32), seq_len, 0)
        weights = lax.dynamic_index_in_dim(taps, offset, 0, keepdims=True)
        return running + weights * window

    return lax.fori_loop(0, tap_count, add_tap, jnp.zeros_like(signal))


def reference(query_stream, key_stream, value_stream, feat_taps, filt_taps, skip_bias, out_weight):
    query_feat = causal_conv(query_stream.astype(jnp.float32), feat_taps[0])
    key_feat = causal_conv(key_stream.astype(jnp.float32), feat_taps[1])
    value_feat = causal_conv(value_stream.astype(jnp.float32), feat_taps[2])
    gated = (key_feat * value_feat).astype(jnp.bfloat16)
    gated_wide = gated.astype(jnp.float32)
    mixed = causal_conv(gated_wide, filt_taps) + skip_bias[None, :] * gated_wide
    product = (query_feat * mixed).astype(jnp.bfloat16)
    group_width = D // N_TP

    def add_group(running, group):
        columns = lax.dynamic_slice_in_dim(product, group * group_width, group_width, 1)
        weights = lax.dynamic_slice_in_dim(out_weight, group * group_width, group_width, 0)
        partial_sum = jnp.dot(columns, weights, preferred_element_type=jnp.float32).astype(jnp.bfloat16)
        partial_sum = lax.optimization_barrier(partial_sum)
        return running + partial_sum.astype(jnp.float32), None

    summed, unused = lax.scan(add_group, jnp.zeros((product.shape[0], out_weight.shape[1]), jnp.float32), jnp.arange(N_TP, dtype=jnp.int32))
    return summed.astype(jnp.bfloat16)
```

```python
import jax
import jax.numpy as jnp
from jax import lax
from jax.sharding import PartitionSpec as P


def shifted(block, axis, distance):
    devices = range(lax.axis_size(axis))
    route = [(i - distance, i) for i in devices if i - distance in devices]
    return lax.ppermute(block, axis, route)


def valid_conv(extended, taps):
    tap_count = taps.shape[0]
    out_rows = extended.shape[0] - tap_count + 1
    running = taps[0][None, :] * extended[tap_count - 1 : tap_count - 1 + out_rows]
    for offset in range(1, tap_count):
        running = (
            running
            + taps[offset][None, :]
            * extended[tap_count - 1 - offset : tap_count - 1 - offset + out_rows]
        )
    return running


def line_reduce_scatter(terms, axis):
    n = lax.axis_size(axis)
    me = lax.axis_index(axis)
    width = terms.shape[1] // n

    def block(j):
        j = jnp.clip(j, 0, n - 1)
        return lax.dynamic_slice_in_dim(terms, j * width, width, 1).astype(jnp.float32)

    zeros = jnp.zeros((terms.shape[0], width), terms.dtype)
    from_left, from_right = zeros, zeros
    for step in range(n - 1):
        send_right = (from_left.astype(jnp.float32) + block(n - 1 + me - step)).astype(terms.dtype)
        send_left = (from_right.astype(jnp.float32) + block(step - (n - 1) + me)).astype(terms.dtype)
        from_left = lax.ppermute(send_right, axis, [(k, k + 1) for k in range(n - 1) if k <= step])
        from_right = lax.ppermute(send_left, axis, [(k, k - 1) for k in range(1, n) if k >= n - 1 - step])
    total = from_left.astype(jnp.float32) + block(me) + from_right.astype(jnp.float32)
    return total.astype(terms.dtype)


def shards(query_stream, key_stream, value_stream, feat_taps, filt_taps, skip_bias, out_weight):
    filt_reach = filt_taps.shape[0] - 1
    feat_reach = feat_taps.shape[1] - 1
    full_reach = filt_reach + feat_reach
    outgoing = jnp.concatenate(
        [key_stream[-full_reach:], value_stream[-full_reach:], query_stream[-feat_reach:]], 0
    )
    incoming = shifted(outgoing, "ctx", 1)
    key_ext = jnp.concatenate([incoming[:full_reach], key_stream], 0)
    value_ext = jnp.concatenate([incoming[full_reach : 2 * full_reach], value_stream], 0)
    query_ext = jnp.concatenate([incoming[2 * full_reach :], query_stream], 0)
    key_feat = valid_conv(key_ext.astype(jnp.float32), feat_taps[1])
    value_feat = valid_conv(value_ext.astype(jnp.float32), feat_taps[2])
    query_feat = valid_conv(query_ext.astype(jnp.float32), feat_taps[0])
    gated = (key_feat * value_feat).astype(jnp.bfloat16)
    own_gated = gated[filt_reach:].astype(jnp.float32)
    mixed = valid_conv(gated.astype(jnp.float32), filt_taps) + skip_bias[None, :] * own_gated
    product = (query_feat * mixed).astype(jnp.bfloat16)
    terms = jnp.dot(product, out_weight, preferred_element_type=jnp.float32)
    return line_reduce_scatter(terms.astype(jnp.bfloat16), "tp")


def solution(mesh):
    in_specs = (
        P("ctx", "tp"),
        P("ctx", "tp"),
        P("ctx", "tp"),
        P(None, None, "tp"),
        P(None, "tp"),
        P("tp"),
        P("tp", None),
    )
    out_specs = P("ctx", "tp")
    return jax.shard_map(shards, mesh=mesh, in_specs=in_specs, out_specs=out_specs, check_vma=False)
```

```python
import jax
import jax.numpy as jnp
from jax import lax
from jax.sharding import PartitionSpec as P


def shifted(block, axis, distance):
    devices = range(lax.axis_size(axis))
    route = [(i - distance, i) for i in devices if i - distance in devices]
    return lax.ppermute(block, axis, route)


def valid_conv(extended, taps):
    tap_count = taps.shape[0]
    out_rows = extended.shape[0] - tap_count + 1
    running = taps[0][None, :] * extended[tap_count - 1 : tap_count - 1 + out_rows]
    for offset in range(1, tap_count):
        running = (
            running
            + taps[offset][None, :]
            * extended[tap_count - 1 - offset : tap_count - 1 - offset + out_rows]
        )
    return running


def line_reduce_scatter(product, out_weight, axis, chains=2):
    n = lax.axis_size(axis)
    me = lax.axis_index(axis)
    width = out_weight.shape[1] // n
    piece = width // chains

    def block(j, chain):
        j = jnp.clip(j, 0, n - 1)
        columns = lax.dynamic_slice_in_dim(out_weight, j * width + chain * piece, piece, 1)
        term = jnp.dot(product, columns, preferred_element_type=jnp.float32)
        return term.astype(jnp.bfloat16).astype(jnp.float32)

    zeros = jnp.zeros((product.shape[0], piece), jnp.bfloat16)
    from_left = [zeros] * chains
    from_right = [zeros] * chains
    for step in range(n - 1):
        rightward = [(k, k + 1) for k in range(n - 1) if k <= step]
        leftward = [(k, k - 1) for k in range(1, n) if k >= n - 1 - step]
        for chain in range(chains):
            send_right = (from_left[chain].astype(jnp.float32) + block(n - 1 + me - step, chain)).astype(jnp.bfloat16)
            send_left = (from_right[chain].astype(jnp.float32) + block(step - (n - 1) + me, chain)).astype(jnp.bfloat16)
            from_left[chain] = lax.ppermute(send_right, axis, rightward)
            from_right[chain] = lax.ppermute(send_left, axis, leftward)
    pieces = [
        from_left[chain].astype(jnp.float32) + block(me, chain) + from_right[chain].astype(jnp.float32)
        for chain in range(chains)
    ]
    return jnp.concatenate(pieces, 1).astype(jnp.bfloat16)


def shards(query_stream, key_stream, value_stream, feat_taps, filt_taps, skip_bias, out_weight):
    filt_reach = filt_taps.shape[0] - 1
    feat_reach = feat_taps.shape[1] - 1
    full_reach = filt_reach + feat_reach
    outgoing = jnp.concatenate(
        [key_stream[-full_reach:], value_stream[-full_reach:], query_stream[-feat_reach:]], 0
    )
    incoming = shifted(outgoing, "ctx", 1)
    key_ext = jnp.concatenate([incoming[:full_reach], key_stream], 0)
    value_ext = jnp.concatenate([incoming[full_reach : 2 * full_reach], value_stream], 0)
    query_ext = jnp.concatenate([incoming[2 * full_reach :], query_stream], 0)
    key_feat = valid_conv(key_ext.astype(jnp.float32), feat_taps[1])
    value_feat = valid_conv(value_ext.astype(jnp.float32), feat_taps[2])
    query_feat = valid_conv(query_ext.astype(jnp.float32), feat_taps[0])
    gated = (key_feat * value_feat).astype(jnp.bfloat16)
    own_gated = gated[filt_reach:].astype(jnp.float32)
    mixed = valid_conv(gated.astype(jnp.float32), filt_taps) + skip_bias[None, :] * own_gated
    product = (query_feat * mixed).astype(jnp.bfloat16)
    return line_reduce_scatter(product, out_weight, "tp")


def solution(mesh):
    in_specs = (
        P("ctx", "tp"),
        P("ctx", "tp"),
        P("ctx", "tp"),
        P(None, None, "tp"),
        P(None, "tp"),
        P("tp"),
        P("tp", None),
    )
    out_specs = P("ctx", "tp")
    return jax.shard_map(shards, mesh=mesh, in_specs=in_specs, out_specs=out_specs, check_vma=False)
```

```python
import jax
import jax.numpy as jnp
from jax import lax
from jax.sharding import PartitionSpec as P


def shifted(block, axis, distance):
    devices = range(lax.axis_size(axis))
    route = [(i - distance, i) for i in devices if i - distance in devices]
    return lax.ppermute(block, axis, route)


def valid_conv(extended, taps):
    tap_count = taps.shape[0]
    out_rows = extended.shape[0] - tap_count + 1
    running = taps[0][None, :] * extended[tap_count - 1 : tap_count - 1 + out_rows]
    for offset in range(1, tap_count):
        running = (
            running
            + taps[offset][None, :]
            * extended[tap_count - 1 - offset : tap_count - 1 - offset + out_rows]
        )
    return running


def line_reduce_scatter(product, out_weight, axis, chains=1):
    n = lax.axis_size(axis)
    me = lax.axis_index(axis)
    width = out_weight.shape[1] // n
    piece = width // chains

    def block(j, chain):
        j = jnp.clip(j, 0, n - 1)
        columns = lax.dynamic_slice_in_dim(out_weight, j * width + chain * piece, piece, 1)
        term = jnp.dot(product, columns, preferred_element_type=jnp.float32)
        return term.astype(jnp.bfloat16).astype(jnp.float32)

    zeros = jnp.zeros((product.shape[0], piece), jnp.bfloat16)
    from_left = [zeros] * chains
    from_right = [zeros] * chains
    for step in range(n - 1):
        rightward = [(k, k + 1) for k in range(n - 1) if k <= step]
        leftward = [(k, k - 1) for k in range(1, n) if k >= n - 1 - step]
        for chain in range(chains):
            send_right = (from_left[chain].astype(jnp.float32) + block(n - 1 + me - step, chain)).astype(jnp.bfloat16)
            send_left = (from_right[chain].astype(jnp.float32) + block(step - (n - 1) + me, chain)).astype(jnp.bfloat16)
            from_left[chain] = lax.ppermute(send_right, axis, rightward)
            from_right[chain] = lax.ppermute(send_left, axis, leftward)
    pieces = [
        from_left[chain].astype(jnp.float32) + block(me, chain) + from_right[chain].astype(jnp.float32)
        for chain in range(chains)
    ]
    return jnp.concatenate(pieces, 1).astype(jnp.bfloat16)


def shards(query_stream, key_stream, value_stream, feat_taps, filt_taps, skip_bias, out_weight):
    filt_reach = filt_taps.shape[0] - 1
    feat_reach = feat_taps.shape[1] - 1
    full_reach = filt_reach + feat_reach
    outgoing = jnp.concatenate(
        [key_stream[-full_reach:], value_stream[-full_reach:], query_stream[-feat_reach:]], 0
    )
    incoming = shifted(outgoing, "ctx", 1)
    key_ext = jnp.concatenate([incoming[:full_reach], key_stream], 0)
    value_ext = jnp.concatenate([incoming[full_reach : 2 * full_reach], value_stream], 0)
    query_ext = jnp.concatenate([incoming[2 * full_reach :], query_stream], 0)
    key_feat = valid_conv(key_ext.astype(jnp.float32), feat_taps[1])
    value_feat = valid_conv(value_ext.astype(jnp.float32), feat_taps[2])
    query_feat = valid_conv(query_ext.astype(jnp.float32), feat_taps[0])
    gated = (key_feat * value_feat).astype(jnp.bfloat16)
    own_gated = gated[filt_reach:].astype(jnp.float32)
    mixed = valid_conv(gated.astype(jnp.float32), filt_taps) + skip_bias[None, :] * own_gated
    product = (query_feat * mixed).astype(jnp.bfloat16)
    return line_reduce_scatter(product, out_weight, "tp")


def solution(mesh):
    in_specs = (
        P("ctx", "tp"),
        P("ctx", "tp"),
        P("ctx", "tp"),
        P(None, None, "tp"),
        P(None, "tp"),
        P("tp"),
        P("tp", None),
    )
    out_specs = P("ctx", "tp")
    return jax.shard_map(shards, mesh=mesh, in_specs=in_specs, out_specs=out_specs, check_vma=False)
```

```python
import jax
import jax.numpy as jnp
from jax import lax
from jax.sharding import PartitionSpec as P


def shifted(block, axis, distance):
    devices = range(lax.axis_size(axis))
    route = [(i - distance, i) for i in devices if i - distance in devices]
    return lax.ppermute(block, axis, route)


def valid_conv(extended, taps):
    tap_count = taps.shape[0]
    out_rows = extended.shape[0] - tap_count + 1
    running = taps[0][None, :] * extended[tap_count - 1 : tap_count - 1 + out_rows]
    for offset in range(1, tap_count):
        running = (
            running
            + taps[offset][None, :]
            * extended[tap_count - 1 - offset : tap_count - 1 - offset + out_rows]
        )
    return running


def line_reduce_scatter(product, out_weight, axis, chains=1):
    n = lax.axis_size(axis)
    me = lax.axis_index(axis)
    width = out_weight.shape[1] // n
    piece = width // chains

    def block(j, chain):
        j = jnp.clip(j, 0, n - 1)
        columns = lax.dynamic_slice_in_dim(out_weight, j * width + chain * piece, piece, 1)
        term = jnp.dot(product, columns, preferred_element_type=jnp.float32)
        return term.astype(jnp.bfloat16).astype(jnp.float32)

    zeros = jnp.zeros((product.shape[0], piece), jnp.bfloat16)
    from_left = [zeros] * chains
    from_right = [zeros] * chains
    for step in range(n - 1):
        rightward = [(k, k + 1) for k in range(n - 1) if k <= step]
        leftward = [(k, k - 1) for k in range(1, n) if k >= n - 1 - step]
        for chain in range(chains):
            send_right = (from_left[chain].astype(jnp.float32) + block(n - 1 + me - step, chain)).astype(jnp.bfloat16)
            send_left = (from_right[chain].astype(jnp.float32) + block(step - (n - 1) + me, chain)).astype(jnp.bfloat16)
            from_left[chain] = lax.ppermute(send_right, axis, rightward)
            from_right[chain] = lax.ppermute(send_left, axis, leftward)
    pieces = [
        from_left[chain].astype(jnp.float32) + block(me, chain) + from_right[chain].astype(jnp.float32)
        for chain in range(chains)
    ]
    return jnp.concatenate(pieces, 1).astype(jnp.bfloat16)


def shards(query_stream, key_stream, value_stream, feat_taps, filt_taps, skip_bias, out_weight):
    filt_reach = filt_taps.shape[0] - 1
    feat_reach = feat_taps.shape[1] - 1
    wide = lambda x: x.astype(jnp.float32)
    key_body = valid_conv(wide(key_stream), feat_taps[1])
    value_body = valid_conv(wide(value_stream), feat_taps[2])
    gated_body = (key_body * value_body).astype(jnp.bfloat16)
    outgoing = jnp.concatenate(
        [gated_body[-filt_reach:], key_stream[-feat_reach:], value_stream[-feat_reach:], query_stream[-feat_reach:]], 0
    )
    incoming = shifted(outgoing, "ctx", 1)
    gated_halo = incoming[:filt_reach]
    key_halo = incoming[filt_reach : filt_reach + feat_reach]
    value_halo = incoming[filt_reach + feat_reach : filt_reach + 2 * feat_reach]
    query_halo = incoming[filt_reach + 2 * feat_reach :]
    key_head = valid_conv(wide(jnp.concatenate([key_halo, key_stream[:feat_reach]], 0)), feat_taps[1])
    value_head = valid_conv(wide(jnp.concatenate([value_halo, value_stream[:feat_reach]], 0)), feat_taps[2])
    gated_head = (key_head * value_head).astype(jnp.bfloat16)
    gated = jnp.concatenate([gated_halo, gated_head, gated_body], 0)
    query_feat = valid_conv(wide(jnp.concatenate([query_halo, query_stream], 0)), feat_taps[0])
    own_gated = wide(gated[filt_reach:])
    mixed = valid_conv(wide(gated), filt_taps) + skip_bias[None, :] * own_gated
    product = (query_feat * mixed).astype(jnp.bfloat16)
    return line_reduce_scatter(product, out_weight, "tp")


def solution(mesh):
    in_specs = (
        P("ctx", "tp"),
        P("ctx", "tp"),
        P("ctx", "tp"),
        P(None, None, "tp"),
        P(None, "tp"),
        P("tp"),
        P("tp", None),
    )
    out_specs = P("ctx", "tp")
    return jax.shard_map(shards, mesh=mesh, in_specs=in_specs, out_specs=out_specs, check_vma=False)
```

```python
import jax
import jax.numpy as jnp
from jax import lax
from jax.sharding import PartitionSpec as P


def shifted(block, axis, distance):
    devices = range(lax.axis_size(axis))
    route = [(i - distance, i) for i in devices if i - distance in devices]
    return lax.ppermute(block, axis, route)


def valid_conv(extended, taps):
    tap_count = taps.shape[0]
    out_rows = extended.shape[0] - tap_count + 1
    running = taps[0][None, :] * extended[tap_count - 1 : tap_count - 1 + out_rows]
    for offset in range(1, tap_count):
        running = (
            running
            + taps[offset][None, :]
            * extended[tap_count - 1 - offset : tap_count - 1 - offset + out_rows]
        )
    return running


def line_reduce_scatter(product, out_weight, axis, chains=1):
    n = lax.axis_size(axis)
    me = lax.axis_index(axis)
    width = out_weight.shape[1] // n
    piece = width // chains

    def block(j, chain):
        j = jnp.clip(j, 0, n - 1)
        columns = lax.dynamic_slice_in_dim(out_weight, j * width + chain * piece, piece, 1)
        term = jnp.dot(product, columns, preferred_element_type=jnp.float32)
        return term.astype(jnp.bfloat16).astype(jnp.float32)

    zeros = jnp.zeros((product.shape[0], piece), jnp.bfloat16)
    from_left = [zeros] * chains
    from_right = [zeros] * chains
    for step in range(n - 1):
        rightward = [(k, k + 1) for k in range(n - 1) if k <= step]
        leftward = [(k, k - 1) for k in range(1, n) if k >= n - 1 - step]
        for chain in range(chains):
            send_right = (from_left[chain].astype(jnp.float32) + block(n - 1 + me - step, chain)).astype(jnp.bfloat16)
            send_left = (from_right[chain].astype(jnp.float32) + block(step - (n - 1) + me, chain)).astype(jnp.bfloat16)
            from_left[chain] = lax.ppermute(send_right, axis, rightward)
            from_right[chain] = lax.ppermute(send_left, axis, leftward)
    pieces = [
        from_left[chain].astype(jnp.float32) + block(me, chain) + from_right[chain].astype(jnp.float32)
        for chain in range(chains)
    ]
    return jnp.concatenate(pieces, 1).astype(jnp.bfloat16)


def shards(query_stream, key_stream, value_stream, feat_taps, filt_taps, skip_bias, out_weight):
    filt_reach = filt_taps.shape[0] - 1
    feat_reach = feat_taps.shape[1] - 1
    full_reach = filt_reach + feat_reach
    wide = lambda x: x.astype(jnp.float32)
    key_body = valid_conv(wide(key_stream), feat_taps[1])
    value_body = valid_conv(wide(value_stream), feat_taps[2])
    gated_body = (key_body * value_body).astype(jnp.bfloat16)
    outgoing = jnp.concatenate(
        [gated_body[-filt_reach:], key_stream[-feat_reach:], value_stream[-feat_reach:], query_stream[-feat_reach:]], 0
    )
    incoming = shifted(outgoing, "ctx", 1)
    query_body = valid_conv(wide(query_stream), feat_taps[0])
    mixed_tail = valid_conv(wide(gated_body), filt_taps) + skip_bias[None, :] * wide(gated_body[filt_reach:])
    product_tail = (query_body[filt_reach:] * mixed_tail).astype(jnp.bfloat16)
    gated_halo = incoming[:filt_reach]
    key_halo = incoming[filt_reach : filt_reach + feat_reach]
    value_halo = incoming[filt_reach + feat_reach : filt_reach + 2 * feat_reach]
    query_halo = incoming[filt_reach + 2 * feat_reach :]
    key_head = valid_conv(wide(jnp.concatenate([key_halo, key_stream[:feat_reach]], 0)), feat_taps[1])
    value_head = valid_conv(wide(jnp.concatenate([value_halo, value_stream[:feat_reach]], 0)), feat_taps[2])
    gated_head = (key_head * value_head).astype(jnp.bfloat16)
    query_head = valid_conv(wide(jnp.concatenate([query_halo, query_stream[:feat_reach]], 0)), feat_taps[0])
    gated = jnp.concatenate([gated_halo, gated_head, gated_body[: full_reach - feat_reach]], 0)
    own_gated = wide(gated[filt_reach:])
    mixed_head = valid_conv(wide(gated), filt_taps) + skip_bias[None, :] * own_gated
    query_feat_head = jnp.concatenate([query_head, query_body[: full_reach - feat_reach]], 0)
    product_head = (query_feat_head * mixed_head).astype(jnp.bfloat16)
    product = jnp.concatenate([product_head, product_tail], 0)
    return line_reduce_scatter(product, out_weight, "tp")


def solution(mesh):
    in_specs = (
        P("ctx", "tp"),
        P("ctx", "tp"),
        P("ctx", "tp"),
        P(None, None, "tp"),
        P(None, "tp"),
        P("tp"),
        P("tp", None),
    )
    out_specs = P("ctx", "tp")
    return jax.shard_map(shards, mesh=mesh, in_specs=in_specs, out_specs=out_specs, check_vma=False)
```

```python
import jax
import jax.numpy as jnp
from jax import lax
from jax.sharding import PartitionSpec as P


def shifted(block, axis, distance):
    devices = range(lax.axis_size(axis))
    route = [(i - distance, i) for i in devices if i - distance in devices]
    return lax.ppermute(block, axis, route)


def valid_conv(extended, taps):
    tap_count = taps.shape[0]
    out_rows = extended.shape[0] - tap_count + 1
    running = taps[0][None, :] * extended[tap_count - 1 : tap_count - 1 + out_rows]
    for offset in range(1, tap_count):
        running = (
            running
            + taps[offset][None, :]
            * extended[tap_count - 1 - offset : tap_count - 1 - offset + out_rows]
        )
    return running


def line_reduce_scatter(product, out_weight, axis, chains=1):
    n = lax.axis_size(axis)
    me = lax.axis_index(axis)
    width = out_weight.shape[1] // n
    piece = width // chains

    def block(j, chain):
        j = jnp.clip(j, 0, n - 1)
        columns = lax.dynamic_slice_in_dim(out_weight, j * width + chain * piece, piece, 1)
        term = jnp.dot(product, columns, preferred_element_type=jnp.float32).astype(jnp.bfloat16)
        return lax.optimization_barrier(term).astype(jnp.float32)

    zeros = jnp.zeros((product.shape[0], piece), jnp.bfloat16)
    from_left = [zeros] * chains
    from_right = [zeros] * chains
    for step in range(n - 1):
        rightward = [(k, k + 1) for k in range(n - 1) if k <= step]
        leftward = [(k, k - 1) for k in range(1, n) if k >= n - 1 - step]
        for chain in range(chains):
            send_right = (from_left[chain].astype(jnp.float32) + block(n - 1 + me - step, chain)).astype(jnp.bfloat16)
            send_left = (from_right[chain].astype(jnp.float32) + block(step - (n - 1) + me, chain)).astype(jnp.bfloat16)
            from_left[chain] = lax.ppermute(send_right, axis, rightward)
            from_right[chain] = lax.ppermute(send_left, axis, leftward)
    pieces = [
        from_left[chain].astype(jnp.float32) + block(me, chain) + from_right[chain].astype(jnp.float32)
        for chain in range(chains)
    ]
    return jnp.concatenate(pieces, 1).astype(jnp.bfloat16)


def shards(query_stream, key_stream, value_stream, feat_taps, filt_taps, skip_bias, out_weight):
    filt_reach = filt_taps.shape[0] - 1
    feat_reach = feat_taps.shape[1] - 1
    full_reach = filt_reach + feat_reach
    wide = lambda x: x.astype(jnp.float32)
    key_body = valid_conv(wide(key_stream), feat_taps[1])
    value_body = valid_conv(wide(value_stream), feat_taps[2])
    gated_body = (key_body * value_body).astype(jnp.bfloat16)
    outgoing = jnp.concatenate(
        [gated_body[-filt_reach:], key_stream[-feat_reach:], value_stream[-feat_reach:], query_stream[-feat_reach:]], 0
    )
    incoming = shifted(outgoing, "ctx", 1)
    query_body = valid_conv(wide(query_stream), feat_taps[0])
    mixed_tail = valid_conv(wide(gated_body), filt_taps) + skip_bias[None, :] * wide(gated_body[filt_reach:])
    product_tail = (query_body[filt_reach:] * mixed_tail).astype(jnp.bfloat16)
    gated_halo = incoming[:filt_reach]
    key_halo = incoming[filt_reach : filt_reach + feat_reach]
    value_halo = incoming[filt_reach + feat_reach : filt_reach + 2 * feat_reach]
    query_halo = incoming[filt_reach + 2 * feat_reach :]
    key_head = valid_conv(wide(jnp.concatenate([key_halo, key_stream[:feat_reach]], 0)), feat_taps[1])
    value_head = valid_conv(wide(jnp.concatenate([value_halo, value_stream[:feat_reach]], 0)), feat_taps[2])
    gated_head = (key_head * value_head).astype(jnp.bfloat16)
    query_head = valid_conv(wide(jnp.concatenate([query_halo, query_stream[:feat_reach]], 0)), feat_taps[0])
    gated = jnp.concatenate([gated_halo, gated_head, gated_body[: full_reach - feat_reach]], 0)
    own_gated = wide(gated[filt_reach:])
    mixed_head = valid_conv(wide(gated), filt_taps) + skip_bias[None, :] * own_gated
    query_feat_head = jnp.concatenate([query_head, query_body[: full_reach - feat_reach]], 0)
    product_head = (query_feat_head * mixed_head).astype(jnp.bfloat16)
    product = jnp.concatenate([product_head, product_tail], 0)
    return line_reduce_scatter(product, out_weight, "tp")


def solution(mesh):
    in_specs = (
        P("ctx", "tp"),
        P("ctx", "tp"),
        P("ctx", "tp"),
        P(None, None, "tp"),
        P(None, "tp"),
        P("tp"),
        P("tp", None),
    )
    out_specs = P("ctx", "tp")
    return jax.shard_map(shards, mesh=mesh, in_specs=in_specs, out_specs=out_specs, check_vma=False)
```

```python
import jax
import jax.numpy as jnp
from jax import lax
from jax.sharding import PartitionSpec as P


def shifted(block, axis, distance):
    devices = range(lax.axis_size(axis))
    route = [(i - distance, i) for i in devices if i - distance in devices]
    return lax.ppermute(block, axis, route)


def valid_conv(extended, taps):
    tap_count = taps.shape[0]
    out_rows = extended.shape[0] - tap_count + 1
    running = taps[0][None, :] * extended[tap_count - 1 : tap_count - 1 + out_rows]
    for offset in range(1, tap_count):
        running = (
            running
            + taps[offset][None, :]
            * extended[tap_count - 1 - offset : tap_count - 1 - offset + out_rows]
        )
    return running


def line_reduce_scatter(product, out_weight, axis, chains=1):
    n = lax.axis_size(axis)
    me = lax.axis_index(axis)
    width = out_weight.shape[1] // n
    piece = width // chains

    def block(j, chain):
        j = jnp.clip(j, 0, n - 1)
        columns = lax.dynamic_slice_in_dim(out_weight, j * width + chain * piece, piece, 1)
        term = jnp.dot(product, columns, preferred_element_type=jnp.float32).astype(jnp.bfloat16)
        return lax.optimization_barrier(term).astype(jnp.float32)

    zeros = jnp.zeros((product.shape[0], piece), jnp.bfloat16)
    from_left = [zeros] * chains
    from_right = [zeros] * chains
    for step in range(n - 1):
        rightward = [(k, k + 1) for k in range(n - 1) if k <= step]
        leftward = [(k, k - 1) for k in range(1, n) if k >= n - 1 - step]
        for chain in range(chains):
            send_right = (from_left[chain].astype(jnp.float32) + block(n - 1 + me - step, chain)).astype(jnp.bfloat16)
            send_left = (from_right[chain].astype(jnp.float32) + block(step - (n - 1) + me, chain)).astype(jnp.bfloat16)
            from_left[chain] = lax.ppermute(send_right, axis, rightward)
            from_right[chain] = lax.ppermute(send_left, axis, leftward)
            from_left[chain], from_right[chain] = lax.optimization_barrier((from_left[chain], from_right[chain]))
    pieces = [
        from_left[chain].astype(jnp.float32) + block(me, chain) + from_right[chain].astype(jnp.float32)
        for chain in range(chains)
    ]
    return jnp.concatenate(pieces, 1).astype(jnp.bfloat16)


def shards(query_stream, key_stream, value_stream, feat_taps, filt_taps, skip_bias, out_weight):
    filt_reach = filt_taps.shape[0] - 1
    feat_reach = feat_taps.shape[1] - 1
    full_reach = filt_reach + feat_reach
    wide = lambda x: x.astype(jnp.float32)
    key_body = valid_conv(wide(key_stream), feat_taps[1])
    value_body = valid_conv(wide(value_stream), feat_taps[2])
    gated_body = (key_body * value_body).astype(jnp.bfloat16)
    outgoing = jnp.concatenate(
        [gated_body[-filt_reach:], key_stream[-feat_reach:], value_stream[-feat_reach:], query_stream[-feat_reach:]], 0
    )
    incoming = shifted(outgoing, "ctx", 1)
    query_body = valid_conv(wide(query_stream), feat_taps[0])
    mixed_tail = valid_conv(wide(gated_body), filt_taps) + skip_bias[None, :] * wide(gated_body[filt_reach:])
    product_tail = (query_body[filt_reach:] * mixed_tail).astype(jnp.bfloat16)
    gated_halo = incoming[:filt_reach]
    key_halo = incoming[filt_reach : filt_reach + feat_reach]
    value_halo = incoming[filt_reach + feat_reach : filt_reach + 2 * feat_reach]
    query_halo = incoming[filt_reach + 2 * feat_reach :]
    key_head = valid_conv(wide(jnp.concatenate([key_halo, key_stream[:feat_reach]], 0)), feat_taps[1])
    value_head = valid_conv(wide(jnp.concatenate([value_halo, value_stream[:feat_reach]], 0)), feat_taps[2])
    gated_head = (key_head * value_head).astype(jnp.bfloat16)
    query_head = valid_conv(wide(jnp.concatenate([query_halo, query_stream[:feat_reach]], 0)), feat_taps[0])
    gated = jnp.concatenate([gated_halo, gated_head, gated_body[: full_reach - feat_reach]], 0)
    own_gated = wide(gated[filt_reach:])
    mixed_head = valid_conv(wide(gated), filt_taps) + skip_bias[None, :] * own_gated
    query_feat_head = jnp.concatenate([query_head, query_body[: full_reach - feat_reach]], 0)
    product_head = (query_feat_head * mixed_head).astype(jnp.bfloat16)
    product = jnp.concatenate([product_head, product_tail], 0)
    return line_reduce_scatter(product, out_weight, "tp")


def solution(mesh):
    in_specs = (
        P("ctx", "tp"),
        P("ctx", "tp"),
        P("ctx", "tp"),
        P(None, None, "tp"),
        P(None, "tp"),
        P("tp"),
        P("tp", None),
    )
    out_specs = P("ctx", "tp")
    return jax.shard_map(shards, mesh=mesh, in_specs=in_specs, out_specs=out_specs, check_vma=False)
```

```python
import jax
import jax.numpy as jnp
from jax import lax
from jax.sharding import PartitionSpec as P


def shifted(block, axis, distance):
    devices = range(lax.axis_size(axis))
    route = [(i - distance, i) for i in devices if i - distance in devices]
    return lax.ppermute(block, axis, route)


def halo_shift(outgoing, axis, other):
    n_ctx, n_tp = lax.axis_size(axis), lax.axis_size(other)
    pairs = [(i - 1, i) for i in range(1, n_ctx)]
    crossing = [i for i in range(1, n_ctx) if i % 2 == 0 and (i // 2) % 2 == 1]
    split = outgoing.shape[0] // 2
    moved_head = lax.ppermute(outgoing[:split], axis, pairs)
    rest = outgoing[split:]
    direct = lax.ppermute(rest, axis, [(a, b) for a, b in pairs if b not in crossing])
    flat = lambda c, t: c * n_tp + t
    first, second = [], []
    for i in crossing:
        for j in range(n_tp):
            relay = flat(i, j + 1) if j + 1 < n_tp else flat(i - 1, 0)
            first.append((flat(i - 1, j), relay))
            second.append((relay, flat(i, j)))
    relayed = lax.ppermute(lax.ppermute(rest, (axis, other), first), (axis, other), second)
    me = lax.axis_index(axis)
    moved_rest = jnp.where((me % 2 == 0) & ((me // 2) % 2 == 1), relayed, direct)
    return jnp.concatenate([moved_head, moved_rest], 0)


def valid_conv(extended, taps):
    tap_count = taps.shape[0]
    out_rows = extended.shape[0] - tap_count + 1
    running = taps[0][None, :] * extended[tap_count - 1 : tap_count - 1 + out_rows]
    for offset in range(1, tap_count):
        running = (
            running
            + taps[offset][None, :]
            * extended[tap_count - 1 - offset : tap_count - 1 - offset + out_rows]
        )
    return running


def line_reduce_scatter(product, out_weight, axis, chains=1):
    n = lax.axis_size(axis)
    me = lax.axis_index(axis)
    width = out_weight.shape[1] // n
    piece = width // chains

    def block(j, chain):
        j = jnp.clip(j, 0, n - 1)
        columns = lax.dynamic_slice_in_dim(out_weight, j * width + chain * piece, piece, 1)
        term = jnp.dot(product, columns, preferred_element_type=jnp.float32).astype(jnp.bfloat16)
        return lax.optimization_barrier(term).astype(jnp.float32)

    zeros = jnp.zeros((product.shape[0], piece), jnp.bfloat16)
    from_left = [zeros] * chains
    from_right = [zeros] * chains
    for step in range(n - 1):
        rightward = [(k, k + 1) for k in range(n - 1) if k <= step]
        leftward = [(k, k - 1) for k in range(1, n) if k >= n - 1 - step]
        for chain in range(chains):
            send_right = (from_left[chain].astype(jnp.float32) + block(n - 1 + me - step, chain)).astype(jnp.bfloat16)
            send_left = (from_right[chain].astype(jnp.float32) + block(step - (n - 1) + me, chain)).astype(jnp.bfloat16)
            from_left[chain] = lax.ppermute(send_right, axis, rightward)
            from_right[chain] = lax.ppermute(send_left, axis, leftward)
    pieces = [
        from_left[chain].astype(jnp.float32) + block(me, chain) + from_right[chain].astype(jnp.float32)
        for chain in range(chains)
    ]
    return jnp.concatenate(pieces, 1).astype(jnp.bfloat16)


def shards(query_stream, key_stream, value_stream, feat_taps, filt_taps, skip_bias, out_weight):
    filt_reach = filt_taps.shape[0] - 1
    feat_reach = feat_taps.shape[1] - 1
    full_reach = filt_reach + feat_reach
    wide = lambda x: x.astype(jnp.float32)
    key_body = valid_conv(wide(key_stream), feat_taps[1])
    value_body = valid_conv(wide(value_stream), feat_taps[2])
    gated_body = (key_body * value_body).astype(jnp.bfloat16)
    outgoing = jnp.concatenate(
        [gated_body[-filt_reach:], key_stream[-feat_reach:], value_stream[-feat_reach:], query_stream[-feat_reach:]], 0
    )
    incoming = halo_shift(outgoing, "ctx", "tp")
    query_body = valid_conv(wide(query_stream), feat_taps[0])
    mixed_tail = valid_conv(wide(gated_body), filt_taps) + skip_bias[None, :] * wide(gated_body[filt_reach:])
    product_tail = (query_body[filt_reach:] * mixed_tail).astype(jnp.bfloat16)
    gated_halo = incoming[:filt_reach]
    key_halo = incoming[filt_reach : filt_reach + feat_reach]
    value_halo = incoming[filt_reach + feat_reach : filt_reach + 2 * feat_reach]
    query_halo = incoming[filt_reach + 2 * feat_reach :]
    key_head = valid_conv(wide(jnp.concatenate([key_halo, key_stream[:feat_reach]], 0)), feat_taps[1])
    value_head = valid_conv(wide(jnp.concatenate([value_halo, value_stream[:feat_reach]], 0)), feat_taps[2])
    gated_head = (key_head * value_head).astype(jnp.bfloat16)
    query_head = valid_conv(wide(jnp.concatenate([query_halo, query_stream[:feat_reach]], 0)), feat_taps[0])
    gated = jnp.concatenate([gated_halo, gated_head, gated_body[: full_reach - feat_reach]], 0)
    own_gated = wide(gated[filt_reach:])
    mixed_head = valid_conv(wide(gated), filt_taps) + skip_bias[None, :] * own_gated
    query_feat_head = jnp.concatenate([query_head, query_body[: full_reach - feat_reach]], 0)
    product_head = (query_feat_head * mixed_head).astype(jnp.bfloat16)
    product = jnp.concatenate([product_head, product_tail], 0)
    return line_reduce_scatter(product, out_weight, "tp")


def solution(mesh):
    in_specs = (
        P("ctx", "tp"),
        P("ctx", "tp"),
        P("ctx", "tp"),
        P(None, None, "tp"),
        P(None, "tp"),
        P("tp"),
        P("tp", None),
    )
    out_specs = P("ctx", "tp")
    return jax.shard_map(shards, mesh=mesh, in_specs=in_specs, out_specs=out_specs, check_vma=False)
```

```python
import jax
import jax.numpy as jnp
from jax import lax
from jax.sharding import PartitionSpec as P


def shifted(block, axis, distance):
    devices = range(lax.axis_size(axis))
    route = [(i - distance, i) for i in devices if i - distance in devices]
    return lax.ppermute(block, axis, route)


def valid_conv(extended, taps):
    tap_count = taps.shape[0]
    out_rows = extended.shape[0] - tap_count + 1
    running = taps[0][None, :] * extended[tap_count - 1 : tap_count - 1 + out_rows]
    for offset in range(1, tap_count):
        running = (
            running
            + taps[offset][None, :]
            * extended[tap_count - 1 - offset : tap_count - 1 - offset + out_rows]
        )
    return running


def line_reduce_scatter(product, out_weight, axis, chains=1):
    n = lax.axis_size(axis)
    me = lax.axis_index(axis)
    width = out_weight.shape[1] // n
    piece = width // chains

    def block(j, chain):
        j = jnp.clip(j, 0, n - 1)
        columns = lax.dynamic_slice_in_dim(out_weight, j * width + chain * piece, piece, 1)
        term = jnp.dot(product, columns, preferred_element_type=jnp.float32).astype(jnp.bfloat16)
        return lax.optimization_barrier(term).astype(jnp.float32)

    zeros = jnp.zeros((product.shape[0], piece), jnp.bfloat16)
    from_left = [zeros] * chains
    from_right = [zeros] * chains
    for step in range(n - 1):
        rightward = [(k, k + 1) for k in range(n - 1) if k <= step]
        leftward = [(k, k - 1) for k in range(1, n) if k >= n - 1 - step]
        for chain in range(chains):
            send_right = (from_left[chain].astype(jnp.float32) + block(n - 1 + me - step, chain)).astype(jnp.bfloat16)
            send_left = (from_right[chain].astype(jnp.float32) + block(step - (n - 1) + me, chain)).astype(jnp.bfloat16)
            from_left[chain] = lax.ppermute(send_right, axis, rightward)
            from_right[chain] = lax.ppermute(send_left, axis, leftward)
    pieces = [
        from_left[chain].astype(jnp.float32) + block(me, chain) + from_right[chain].astype(jnp.float32)
        for chain in range(chains)
    ]
    return jnp.concatenate(pieces, 1).astype(jnp.bfloat16)


def shards(query_stream, key_stream, value_stream, feat_taps, filt_taps, skip_bias, out_weight):
    filt_reach = filt_taps.shape[0] - 1
    feat_reach = feat_taps.shape[1] - 1
    full_reach = filt_reach + feat_reach
    wide = lambda x: x.astype(jnp.float32)
    key_body = valid_conv(wide(key_stream), feat_taps[1])
    value_body = valid_conv(wide(value_stream), feat_taps[2])
    gated_body = (key_body * value_body).astype(jnp.bfloat16)
    outgoing = jnp.concatenate(
        [gated_body[-filt_reach:], key_stream[-feat_reach:], value_stream[-feat_reach:], query_stream[-feat_reach:]], 0
    )
    query_body = valid_conv(wide(query_stream), feat_taps[0])
    mixed_tail = valid_conv(wide(gated_body), filt_taps) + skip_bias[None, :] * wide(gated_body[filt_reach:])
    product_tail = (query_body[filt_reach:] * mixed_tail).astype(jnp.bfloat16)
    outgoing, product_tail = lax.optimization_barrier((outgoing, product_tail))
    incoming = shifted(outgoing, "ctx", 1)
    gated_halo = incoming[:filt_reach]
    key_halo = incoming[filt_reach : filt_reach + feat_reach]
    value_halo = incoming[filt_reach + feat_reach : filt_reach + 2 * feat_reach]
    query_halo = incoming[filt_reach + 2 * feat_reach :]
    key_head = valid_conv(wide(jnp.concatenate([key_halo, key_stream[:feat_reach]], 0)), feat_taps[1])
    value_head = valid_conv(wide(jnp.concatenate([value_halo, value_stream[:feat_reach]], 0)), feat_taps[2])
    gated_head = (key_head * value_head).astype(jnp.bfloat16)
    query_head = valid_conv(wide(jnp.concatenate([query_halo, query_stream[:feat_reach]], 0)), feat_taps[0])
    gated = jnp.concatenate([gated_halo, gated_head, gated_body[: full_reach - feat_reach]], 0)
    own_gated = wide(gated[filt_reach:])
    mixed_head = valid_conv(wide(gated), filt_taps) + skip_bias[None, :] * own_gated
    query_feat_head = jnp.concatenate([query_head, query_body[: full_reach - feat_reach]], 0)
    product_head = (query_feat_head * mixed_head).astype(jnp.bfloat16)
    product = jnp.concatenate([product_head, product_tail], 0)
    return line_reduce_scatter(product, out_weight, "tp")


def solution(mesh):
    in_specs = (
        P("ctx", "tp"),
        P("ctx", "tp"),
        P("ctx", "tp"),
        P(None, None, "tp"),
        P(None, "tp"),
        P("tp"),
        P("tp", None),
    )
    out_specs = P("ctx", "tp")
    return jax.shard_map(shards, mesh=mesh, in_specs=in_specs, out_specs=out_specs, check_vma=False)
```

```python
import jax
import jax.numpy as jnp
from jax import lax
from jax.sharding import PartitionSpec as P


def shifted(block, axis, distance):
    devices = range(lax.axis_size(axis))
    route = [(i - distance, i) for i in devices if i - distance in devices]
    return lax.ppermute(block, axis, route)


def valid_conv(extended, taps):
    tap_count = taps.shape[0]
    out_rows = extended.shape[0] - tap_count + 1
    running = taps[0][None, :] * extended[tap_count - 1 : tap_count - 1 + out_rows]
    for offset in range(1, tap_count):
        running = (
            running
            + taps[offset][None, :]
            * extended[tap_count - 1 - offset : tap_count - 1 - offset + out_rows]
        )
    return running


def line_reduce_scatter(product, out_weight, axis, chains=1):
    n = lax.axis_size(axis)
    me = lax.axis_index(axis)
    width = out_weight.shape[1] // n
    piece = width // chains

    def block(j, chain):
        j = jnp.clip(j, 0, n - 1)
        columns = lax.dynamic_slice_in_dim(out_weight, j * width + chain * piece, piece, 1)
        term = jnp.dot(product, columns, preferred_element_type=jnp.float32).astype(jnp.bfloat16)
        return lax.optimization_barrier(term).astype(jnp.float32)

    zeros = jnp.zeros((product.shape[0], piece), jnp.bfloat16)
    from_left = [zeros] * chains
    from_right = [zeros] * chains
    for step in range(n - 1):
        rightward = [(k, k + 1) for k in range(n - 1) if k <= step]
        leftward = [(k, k - 1) for k in range(1, n) if k >= n - 1 - step]
        for chain in range(chains):
            send_right = (from_left[chain].astype(jnp.float32) + block(n - 1 + me - step, chain)).astype(jnp.bfloat16)
            send_left = (from_right[chain].astype(jnp.float32) + block(step - (n - 1) + me, chain)).astype(jnp.bfloat16)
            from_left[chain] = lax.ppermute(send_right, axis, rightward)
            from_right[chain] = lax.ppermute(send_left, axis, leftward)
    pieces = [
        from_left[chain].astype(jnp.float32) + block(me, chain) + from_right[chain].astype(jnp.float32)
        for chain in range(chains)
    ]
    return jnp.concatenate(pieces, 1).astype(jnp.bfloat16)


def shards(query_stream, key_stream, value_stream, feat_taps, filt_taps, skip_bias, out_weight):
    filt_reach = filt_taps.shape[0] - 1
    feat_reach = feat_taps.shape[1] - 1
    full_reach = filt_reach + feat_reach
    wide = lambda x: x.astype(jnp.float32)
    key_body = valid_conv(wide(key_stream), feat_taps[1])
    value_body = valid_conv(wide(value_stream), feat_taps[2])
    gated_body = (key_body * value_body).astype(jnp.bfloat16)
    key_last = valid_conv(wide(key_stream[-full_reach:]), feat_taps[1])
    value_last = valid_conv(wide(value_stream[-full_reach:]), feat_taps[2])
    gated_last = (key_last * value_last).astype(jnp.bfloat16)
    outgoing = jnp.concatenate(
        [gated_last, key_stream[-feat_reach:], value_stream[-feat_reach:], query_stream[-feat_reach:]], 0
    )
    incoming = shifted(outgoing, "ctx", 1)
    query_body = valid_conv(wide(query_stream), feat_taps[0])
    mixed_tail = valid_conv(wide(gated_body), filt_taps) + skip_bias[None, :] * wide(gated_body[filt_reach:])
    product_tail = (query_body[filt_reach:] * mixed_tail).astype(jnp.bfloat16)
    gated_halo = incoming[:filt_reach]
    key_halo = incoming[filt_reach : filt_reach + feat_reach]
    value_halo = incoming[filt_reach + feat_reach : filt_reach + 2 * feat_reach]
    query_halo = incoming[filt_reach + 2 * feat_reach :]
    key_head = valid_conv(wide(jnp.concatenate([key_halo, key_stream[:feat_reach]], 0)), feat_taps[1])
    value_head = valid_conv(wide(jnp.concatenate([value_halo, value_stream[:feat_reach]], 0)), feat_taps[2])
    gated_head = (key_head * value_head).astype(jnp.bfloat16)
    query_head = valid_conv(wide(jnp.concatenate([query_halo, query_stream[:feat_reach]], 0)), feat_taps[0])
    gated = jnp.concatenate([gated_halo, gated_head, gated_body[: full_reach - feat_reach]], 0)
    own_gated = wide(gated[filt_reach:])
    mixed_head = valid_conv(wide(gated), filt_taps) + skip_bias[None, :] * own_gated
    query_feat_head = jnp.concatenate([query_head, query_body[: full_reach - feat_reach]], 0)
    product_head = (query_feat_head * mixed_head).astype(jnp.bfloat16)
    product = jnp.concatenate([product_head, product_tail], 0)
    return line_reduce_scatter(product, out_weight, "tp")


def solution(mesh):
    in_specs = (
        P("ctx", "tp"),
        P("ctx", "tp"),
        P("ctx", "tp"),
        P(None, None, "tp"),
        P(None, "tp"),
        P("tp"),
        P("tp", None),
    )
    out_specs = P("ctx", "tp")
    return jax.shard_map(shards, mesh=mesh, in_specs=in_specs, out_specs=out_specs, check_vma=False)
```

```python
import jax
import jax.numpy as jnp
from jax import lax
from jax.sharding import PartitionSpec as P


def shifted(block, axis, distance):
    devices = range(lax.axis_size(axis))
    route = [(i - distance, i) for i in devices if i - distance in devices]
    return lax.ppermute(block, axis, route)


def valid_conv(extended, taps):
    tap_count = taps.shape[0]
    out_rows = extended.shape[0] - tap_count + 1
    running = taps[0][None, :] * extended[tap_count - 1 : tap_count - 1 + out_rows]
    for offset in range(1, tap_count):
        running = (
            running
            + taps[offset][None, :]
            * extended[tap_count - 1 - offset : tap_count - 1 - offset + out_rows]
        )
    return running


def line_reduce_scatter(product, out_weight, axis, chains=2):
    n = lax.axis_size(axis)
    me = lax.axis_index(axis)
    width = out_weight.shape[1] // n
    piece = width // chains

    def block(j, chain):
        j = jnp.clip(j, 0, n - 1)
        columns = lax.dynamic_slice_in_dim(out_weight, j * width + chain * piece, piece, 1)
        term = jnp.dot(product, columns, preferred_element_type=jnp.float32).astype(jnp.bfloat16)
        return lax.optimization_barrier(term).astype(jnp.float32)

    zeros = jnp.zeros((product.shape[0], piece), jnp.bfloat16)
    from_left = [zeros] * chains
    from_right = [zeros] * chains
    all_right = [(k, k + 1) for k in range(n - 1)]
    all_left = [(k, k - 1) for k in range(1, n)]
    for step in range(n - 1):
        rightward = [(k, k + 1) for k in range(n - 1) if k <= step]
        leftward = [(k, k - 1) for k in range(1, n) if k >= n - 1 - step]
        for chain in range(chains):
            send_right = (from_left[chain].astype(jnp.float32) + block(n - 1 + me - step, chain)).astype(jnp.bfloat16)
            send_left = (from_right[chain].astype(jnp.float32) + block(step - (n - 1) + me, chain)).astype(jnp.bfloat16)
            every = chain % 2 == 1
            from_left[chain] = lax.ppermute(send_right, axis, all_right if every else rightward)
            from_right[chain] = lax.ppermute(send_left, axis, all_left if every else leftward)
    pieces = [
        from_left[chain].astype(jnp.float32) + block(me, chain) + from_right[chain].astype(jnp.float32)
        for chain in range(chains)
    ]
    return jnp.concatenate(pieces, 1).astype(jnp.bfloat16)


def shards(query_stream, key_stream, value_stream, feat_taps, filt_taps, skip_bias, out_weight):
    filt_reach = filt_taps.shape[0] - 1
    feat_reach = feat_taps.shape[1] - 1
    full_reach = filt_reach + feat_reach
    wide = lambda x: x.astype(jnp.float32)
    key_body = valid_conv(wide(key_stream), feat_taps[1])
    value_body = valid_conv(wide(value_stream), feat_taps[2])
    gated_body = (key_body * value_body).astype(jnp.bfloat16)
    key_last = valid_conv(wide(key_stream[-full_reach:]), feat_taps[1])
    value_last = valid_conv(wide(value_stream[-full_reach:]), feat_taps[2])
    gated_last = (key_last * value_last).astype(jnp.bfloat16)
    outgoing = jnp.concatenate(
        [gated_last, key_stream[-feat_reach:], value_stream[-feat_reach:], query_stream[-feat_reach:]], 0
    )
    incoming = shifted(outgoing, "ctx", 1)
    query_body = valid_conv(wide(query_stream), feat_taps[0])
    mixed_tail = valid_conv(wide(gated_body), filt_taps) + skip_bias[None, :] * wide(gated_body[filt_reach:])
    product_tail = (query_body[filt_reach:] * mixed_tail).astype(jnp.bfloat16)
    gated_halo = incoming[:filt_reach]
    key_halo = incoming[filt_reach : filt_reach + feat_reach]
    value_halo = incoming[filt_reach + feat_reach : filt_reach + 2 * feat_reach]
    query_halo = incoming[filt_reach + 2 * feat_reach :]
    key_head = valid_conv(wide(jnp.concatenate([key_halo, key_stream[:feat_reach]], 0)), feat_taps[1])
    value_head = valid_conv(wide(jnp.concatenate([value_halo, value_stream[:feat_reach]], 0)), feat_taps[2])
    gated_head = (key_head * value_head).astype(jnp.bfloat16)
    query_head = valid_conv(wide(jnp.concatenate([query_halo, query_stream[:feat_reach]], 0)), feat_taps[0])
    gated = jnp.concatenate([gated_halo, gated_head, gated_body[: full_reach - feat_reach]], 0)
    own_gated = wide(gated[filt_reach:])
    mixed_head = valid_conv(wide(gated), filt_taps) + skip_bias[None, :] * own_gated
    query_feat_head = jnp.concatenate([query_head, query_body[: full_reach - feat_reach]], 0)
    product_head = (query_feat_head * mixed_head).astype(jnp.bfloat16)
    product = jnp.concatenate([product_head, product_tail], 0)
    return line_reduce_scatter(product, out_weight, "tp")


def solution(mesh):
    in_specs = (
        P("ctx", "tp"),
        P("ctx", "tp"),
        P("ctx", "tp"),
        P(None, None, "tp"),
        P(None, "tp"),
        P("tp"),
        P("tp", None),
    )
    out_specs = P("ctx", "tp")
    return jax.shard_map(shards, mesh=mesh, in_specs=in_specs, out_specs=out_specs, check_vma=False)
```

```python
import jax
import jax.numpy as jnp
from jax import lax
from jax.sharding import PartitionSpec as P


def shifted(block, axis, distance):
    devices = range(lax.axis_size(axis))
    route = [(i - distance, i) for i in devices if i - distance in devices]
    return lax.ppermute(block, axis, route)


def valid_conv(extended, taps):
    tap_count = taps.shape[0]
    out_rows = extended.shape[0] - tap_count + 1
    running = taps[0][None, :] * extended[tap_count - 1 : tap_count - 1 + out_rows]
    for offset in range(1, tap_count):
        running = (
            running
            + taps[offset][None, :]
            * extended[tap_count - 1 - offset : tap_count - 1 - offset + out_rows]
        )
    return running


def line_reduce_scatter(product, out_weight, axis, chains=1):
    n = lax.axis_size(axis)
    me = lax.axis_index(axis)
    width = out_weight.shape[1] // n
    piece = width // chains

    def block(j, chain):
        j = jnp.clip(j, 0, n - 1)
        columns = lax.dynamic_slice_in_dim(out_weight, j * width + chain * piece, piece, 1)
        term = jnp.dot(product, columns, preferred_element_type=jnp.float32).astype(jnp.bfloat16)
        return lax.optimization_barrier(term).astype(jnp.float32)

    zeros = jnp.zeros((product.shape[0], piece), jnp.bfloat16)
    from_left = [zeros] * chains
    from_right = [zeros] * chains
    for step in range(n - 1):
        rightward = [(k, k + 1) for k in range(n - 1) if k <= step]
        leftward = [(k, k - 1) for k in range(1, n) if k >= n - 1 - step]
        for chain in range(chains):
            send_right = (from_left[chain].astype(jnp.float32) + block(n - 1 + me - step, chain)).astype(jnp.bfloat16)
            send_left = (from_right[chain].astype(jnp.float32) + block(step - (n - 1) + me, chain)).astype(jnp.bfloat16)
            if step + 1 < n - 2 - step:
                both = lax.ppermute(jnp.where(me <= step, send_right, send_left), axis, rightward + leftward)
                from_left[chain], from_right[chain] = both, both
            else:
                from_left[chain] = lax.ppermute(send_right, axis, rightward)
                from_right[chain] = lax.ppermute(send_left, axis, leftward)
    pieces = [
        from_left[chain].astype(jnp.float32) + block(me, chain) + from_right[chain].astype(jnp.float32)
        for chain in range(chains)
    ]
    return jnp.concatenate(pieces, 1).astype(jnp.bfloat16)


def shards(query_stream, key_stream, value_stream, feat_taps, filt_taps, skip_bias, out_weight):
    filt_reach = filt_taps.shape[0] - 1
    feat_reach = feat_taps.shape[1] - 1
    full_reach = filt_reach + feat_reach
    wide = lambda x: x.astype(jnp.float32)
    key_body = valid_conv(wide(key_stream), feat_taps[1])
    value_body = valid_conv(wide(value_stream), feat_taps[2])
    gated_body = (key_body * value_body).astype(jnp.bfloat16)
    key_last = valid_conv(wide(key_stream[-full_reach:]), feat_taps[1])
    value_last = valid_conv(wide(value_stream[-full_reach:]), feat_taps[2])
    gated_last = (key_last * value_last).astype(jnp.bfloat16)
    outgoing = jnp.concatenate(
        [gated_last, key_stream[-feat_reach:], value_stream[-feat_reach:], query_stream[-feat_reach:]], 0
    )
    incoming = shifted(outgoing, "ctx", 1)
    query_body = valid_conv(wide(query_stream), feat_taps[0])
    mixed_tail = valid_conv(wide(gated_body), filt_taps) + skip_bias[None, :] * wide(gated_body[filt_reach:])
    product_tail = (query_body[filt_reach:] * mixed_tail).astype(jnp.bfloat16)
    gated_halo = incoming[:filt_reach]
    key_halo = incoming[filt_reach : filt_reach + feat_reach]
    value_halo = incoming[filt_reach + feat_reach : filt_reach + 2 * feat_reach]
    query_halo = incoming[filt_reach + 2 * feat_reach :]
    key_head = valid_conv(wide(jnp.concatenate([key_halo, key_stream[:feat_reach]], 0)), feat_taps[1])
    value_head = valid_conv(wide(jnp.concatenate([value_halo, value_stream[:feat_reach]], 0)), feat_taps[2])
    gated_head = (key_head * value_head).astype(jnp.bfloat16)
    query_head = valid_conv(wide(jnp.concatenate([query_halo, query_stream[:feat_reach]], 0)), feat_taps[0])
    gated = jnp.concatenate([gated_halo, gated_head, gated_body[: full_reach - feat_reach]], 0)
    own_gated = wide(gated[filt_reach:])
    mixed_head = valid_conv(wide(gated), filt_taps) + skip_bias[None, :] * own_gated
    query_feat_head = jnp.concatenate([query_head, query_body[: full_reach - feat_reach]], 0)
    product_head = (query_feat_head * mixed_head).astype(jnp.bfloat16)
    product = jnp.concatenate([product_head, product_tail], 0)
    return line_reduce_scatter(product, out_weight, "tp")


def solution(mesh):
    in_specs = (
        P("ctx", "tp"),
        P("ctx", "tp"),
        P("ctx", "tp"),
        P(None, None, "tp"),
        P(None, "tp"),
        P("tp"),
        P("tp", None),
    )
    out_specs = P("ctx", "tp")
    return jax.shard_map(shards, mesh=mesh, in_specs=in_specs, out_specs=out_specs, check_vma=False)
```

```python
import jax
import jax.numpy as jnp
from jax import lax
from jax.sharding import PartitionSpec as P


def shifted(block, axis, distance):
    devices = range(lax.axis_size(axis))
    route = [(i - distance, i) for i in devices if i - distance in devices]
    return lax.ppermute(block, axis, route)


def valid_conv(extended, taps):
    tap_count = taps.shape[0]
    out_rows = extended.shape[0] - tap_count + 1
    rows = lambda start: extended[start : start + out_rows].astype(jnp.float32)
    running = taps[0][None, :] * rows(tap_count - 1)
    for offset in range(1, tap_count):
        running = running + taps[offset][None, :] * rows(tap_count - 1 - offset)
    return running


def line_reduce_scatter(product, out_weight, axis, chains=1):
    n = lax.axis_size(axis)
    me = lax.axis_index(axis)
    width = out_weight.shape[1] // n
    piece = width // chains

    def block(j, chain):
        j = jnp.clip(j, 0, n - 1)
        columns = lax.dynamic_slice_in_dim(out_weight, j * width + chain * piece, piece, 1)
        term = jnp.dot(product, columns, preferred_element_type=jnp.float32).astype(jnp.bfloat16)
        return lax.optimization_barrier(term).astype(jnp.float32)

    zeros = jnp.zeros((product.shape[0], piece), jnp.bfloat16)
    from_left = [zeros] * chains
    from_right = [zeros] * chains
    for step in range(n - 1):
        rightward = [(k, k + 1) for k in range(n - 1) if k <= step]
        leftward = [(k, k - 1) for k in range(1, n) if k >= n - 1 - step]
        for chain in range(chains):
            send_right = (from_left[chain].astype(jnp.float32) + block(n - 1 + me - step, chain)).astype(jnp.bfloat16)
            send_left = (from_right[chain].astype(jnp.float32) + block(step - (n - 1) + me, chain)).astype(jnp.bfloat16)
            from_left[chain] = lax.ppermute(send_right, axis, rightward)
            from_right[chain] = lax.ppermute(send_left, axis, leftward)
    pieces = [
        from_left[chain].astype(jnp.float32) + block(me, chain) + from_right[chain].astype(jnp.float32)
        for chain in range(chains)
    ]
    return jnp.concatenate(pieces, 1).astype(jnp.bfloat16)


def shards(query_stream, key_stream, value_stream, feat_taps, filt_taps, skip_bias, out_weight):
    filt_reach = filt_taps.shape[0] - 1
    feat_reach = feat_taps.shape[1] - 1
    full_reach = filt_reach + feat_reach
    wide = lambda x: x.astype(jnp.float32)
    key_body = valid_conv(key_stream, feat_taps[1])
    value_body = valid_conv(value_stream, feat_taps[2])
    gated_body = (key_body * value_body).astype(jnp.bfloat16)
    key_last = valid_conv(key_stream[-full_reach:], feat_taps[1])
    value_last = valid_conv(value_stream[-full_reach:], feat_taps[2])
    gated_last = (key_last * value_last).astype(jnp.bfloat16)
    outgoing = jnp.concatenate(
        [gated_last, key_stream[-feat_reach:], value_stream[-feat_reach:], query_stream[-feat_reach:]], 0
    )
    incoming = shifted(outgoing, "ctx", 1)
    query_body = valid_conv(query_stream, feat_taps[0])
    mixed_tail = valid_conv(wide(gated_body), filt_taps) + skip_bias[None, :] * wide(gated_body[filt_reach:])
    product_tail = (query_body[filt_reach:] * mixed_tail).astype(jnp.bfloat16)
    gated_halo = incoming[:filt_reach]
    key_halo = incoming[filt_reach : filt_reach + feat_reach]
    value_halo = incoming[filt_reach + feat_reach : filt_reach + 2 * feat_reach]
    query_halo = incoming[filt_reach + 2 * feat_reach :]
    key_head = valid_conv(wide(jnp.concatenate([key_halo, key_stream[:feat_reach]], 0)), feat_taps[1])
    value_head = valid_conv(wide(jnp.concatenate([value_halo, value_stream[:feat_reach]], 0)), feat_taps[2])
    gated_head = (key_head * value_head).astype(jnp.bfloat16)
    query_head = valid_conv(wide(jnp.concatenate([query_halo, query_stream[:feat_reach]], 0)), feat_taps[0])
    gated = jnp.concatenate([gated_halo, gated_head, gated_body[: full_reach - feat_reach]], 0)
    own_gated = wide(gated[filt_reach:])
    mixed_head = valid_conv(wide(gated), filt_taps) + skip_bias[None, :] * own_gated
    query_feat_head = jnp.concatenate([query_head, query_body[: full_reach - feat_reach]], 0)
    product_head = (query_feat_head * mixed_head).astype(jnp.bfloat16)
    product = jnp.concatenate([product_head, product_tail], 0)
    return line_reduce_scatter(product, out_weight, "tp")


def solution(mesh):
    in_specs = (
        P("ctx", "tp"),
        P("ctx", "tp"),
        P("ctx", "tp"),
        P(None, None, "tp"),
        P(None, "tp"),
        P("tp"),
        P("tp", None),
    )
    out_specs = P("ctx", "tp")
    return jax.shard_map(shards, mesh=mesh, in_specs=in_specs, out_specs=out_specs, check_vma=False)
```
